1024 devices in a mesh: rel: 8 (over y, core), vrow: 32 (over z), vcol: 4 (over x).
Axes of the slice: x: 4, y: 4, z: 32, core: 2. Of those that a mesh axis runs over, the one named last changes fastest.
Arguments:
- features: bfloat16 [16384, 1024], P('vrow'), may hold values from -6 to 6
- first_weight: bfloat16 [16, 1024, 512], P('rel'), may hold values from -0.1875 to 0.1875
- first_root: bfloat16 [1024, 512], replicated, may hold values from -0.1875 to 0.1875
- first_bias: float32 [512], replicated, may hold values from -3 to 3
- second_weight: bfloat16 [16, 512, 512], P('rel'), may hold values from -0.25 to 0.25
- second_root: bfloat16 [512, 512], replicated, may hold values from -0.25 to 0.25
- second_bias: float32 [512], replicated, may hold values from -3 to 3
- tiles: bfloat16 [16, 128, 12, 128, 128], P('rel', 'vrow', 'vcol')
- tile_source: int32 [16, 128, 12], P('rel', 'vrow', 'vcol'), may hold values from 0 to 5, as said below
- tile_count: int32 [16, 128, 4], P('rel', 'vrow', 'vcol'), may hold values from 1 to 3, as said below
- send_rows: int32 [8, 32, 4, 256], P('rel', 'vrow', 'vcol'), may hold values from 0 to 511
Outputs:
- embeddings: bfloat16 [32, 512, 512], P('vrow', ('rel', 'vcol'))
The draws below stay inside these ranges and needn't reach their ends.
Inputs may be any that keep to these rules, and one draw needn't show every extreme that they name: `tile_source`: the first of every column group's 3 tile slots names a block of received rows (4 or more). `tile_count`: each relation has a level of its own that bounds its counts; in every draw some block row of some relation fills all 3 slots of every column group.
All inputs are finite; a program needn't handle non-finite values.
Results may differ from the reference program's by a relative error of at most 0.0055.
Values may be sent and summed in bfloat16 or wider, within the bound.
No kernel may reach another device: no remote copies, remote signals or barrier semaphores. Data moves between devices by JAX's collectives and lax.ppermute only.
A program may use at most 32 MiB of HBM per device.

```python
import jax
import jax.numpy as jnp
from jax import lax

F = 1024
HID = 512
RELS = 16
TILES = 12
TB = 128
VDEV = 512
REMOTE = 256
RGROUPS = 8
VROWS = 32
COLS = 4
SPD = 2
TPD = 3
LB = 4
RB = 2
CAP = 8
NB = 128
V = 16384


def draw_tiles(key, part):
    first_key = jax.random.fold_in(key, 0)
    spread = (6.0 / (RELS * TILES * TB)) ** 0.5
    values = jax.random.uniform(first_key, (RELS, NB, TILES, TB, TB), jnp.float32)
    return (values * spread).astype(jnp.bfloat16)


def draw_tile_source(key, part):
    first_key, second_key = jax.random.split(key)
    anywhere = jax.random.randint(first_key, (RELS, NB, TILES), 0, LB + RB)
    received = jax.random.randint(second_key, (RELS, NB, TILES), LB, LB + RB)
    leading = (jnp.arange(TILES) % TPD == 0)[None, None, :]
    return jnp.where(leading, received, anywhere).astype(jnp.int32)


def draw_tile_count(key, part):
    level_key, base_key, rel_key, row_key = jax.random.split(key, 4)
    level = jax.random.randint(level_key, (RELS, 1, 1), 1, TPD + 1)
    base = jax.random.randint(base_key, (RELS, NB, COLS), 0, TPD)
    counts = jnp.minimum(base, level - 1) + 1
    chosen_rel = jax.random.randint(rel_key, (), 0, RELS)
    chosen_row = jax.random.randint(row_key, (), 0, NB)
    struck = (jnp.arange(RELS)[:, None, None] == chosen_rel) & (jnp.arange(NB)[None, :, None] == chosen_row)
    return jnp.where(struck, TPD, counts).astype(jnp.int32)


def with_ends(entries, own_key, smallest, largest):
    spot = [jax.random.randint(jax.random.fold_in(own_key, axis), (), 0, length) for axis, length in enumerate(entries.shape)]
    main_axis = entries.shape.index(max(entries.shape))
    next_to = spot[:main_axis] + [(spot[main_axis] + 1) % entries.shape[main_axis]] + spot[main_axis + 1:]
    return entries.at[tuple(spot)].set(smallest).at[tuple(next_to)].set(largest)


def block_scale(rng, extent, cuts, low, largest):
    factor_of = 1.0
    for axis_at, parts in cuts:
        draws = jax.random.uniform(jax.random.fold_in(jax.random.fold_in(rng, 6), axis_at), (parts,), jnp.float32, low / len(cuts), largest / len(cuts))
        factor_of = factor_of * jnp.repeat(jnp.exp(draws), extent[axis_at] // parts).reshape((-1,) + (1,) * (len(extent) - 1 - axis_at))
    return factor_of


def scatter_about(rng, extent, scale, bound, cuts=(), kind=jnp.bfloat16):
    entries = scale * jax.random.normal(rng, extent, jnp.float32)
    if cuts:
        entries = entries * block_scale(rng, extent, cuts, -0.22, 0.18)
    return jnp.clip(entries, -bound, bound).astype(kind)


def setup_inputs(seed: int = 0) -> dict:
    arg_keys = jax.random.split(jax.random.key(seed), 12)
    features = scatter_about(arg_keys[0], (V, F), 1.0, 6.0, ((0, 32),))
    first_weight = scatter_about(arg_keys[1], (RELS, F, HID), F ** -0.5, 0.1875, ((0, 8),))
    first_root = scatter_about(arg_keys[2], (F, HID), F ** -0.5, 0.1875)
    first_bias = scatter_about(arg_keys[3], (HID,), 0.5, 3.0, (), jnp.float32)
    second_weight = scatter_about(arg_keys[4], (RELS, HID, HID), HID ** -0.5, 0.25, ((0, 8),))
    second_root = scatter_about(arg_keys[5], (HID, HID), HID ** -0.5, 0.25)
    second_bias = scatter_about(arg_keys[6], (HID,), 0.5, 3.0, (), jnp.float32)
    tiles = draw_tiles(jax.random.fold_in(arg_keys[11], 71), 0)
    tile_source = draw_tile_source(jax.random.fold_in(arg_keys[11], 71), 0)
    tile_count = draw_tile_count(jax.random.fold_in(arg_keys[11], 71), 0)
    send_rows = with_ends(jax.random.randint(arg_keys[10], (RGROUPS, VROWS, COLS, REMOTE), 0, VDEV), jax.random.fold_in(arg_keys[10], 1), 0, VDEV - 1).astype(jnp.int32)
    return {"features": features, "first_weight": first_weight, "first_root": first_root, "first_bias": first_bias, "second_weight": second_weight, "second_root": second_root, "second_bias": second_bias, "tiles": tiles, "tile_source": tile_source, "tile_count": tile_count, "send_rows": send_rows}


def source_table(tile_source, tile_count, send_rows):
    offsets = jnp.arange(TB, dtype=jnp.int32)[None, None, None, :]
    block_row = jnp.arange(NB, dtype=jnp.int32)[None, :, None, None]
    slot_index = jnp.arange(TILES, dtype=jnp.int32)
    relation = jnp.arange(RELS, dtype=jnp.int32)[:, None, None, None]
    group_row = block_row // LB
    column = (slot_index // TPD)[None, None, :, None]
    source_block = tile_source[:, :, :, None]
    local_rows = group_row * VDEV + source_block * TB + offsets
    remote_pos = jnp.maximum(source_block - LB, 0) * TB + offsets
    peer = remote_pos // CAP
    within = remote_pos % CAP
    chosen = send_rows[relation // SPD, peer, column, group_row * CAP + within]
    remote_rows = peer * VDEV + chosen
    table = jnp.where(source_block < LB, local_rows, remote_rows).astype(jnp.int32)
    counts = tile_count[:, :, slot_index // TPD]
    live = ((slot_index % TPD)[None, None, :] < counts).astype(jnp.float32)
    return table, live


def layer(inputs, weight, root, bias, tiles, table, live):
    width = weight.shape[2]

    def per_relation(running, pieces):
        one_weight, one_tiles, one_table, one_live = pieces
        projected = jnp.dot(inputs, one_weight, preferred_element_type=jnp.float32).astype(jnp.bfloat16)

        def per_block(block_args):
            tile_group, row_group, live_group = block_args
            picked = projected[row_group].astype(jnp.float32)
            weighted = tile_group.astype(jnp.float32) * live_group[:, :, None, None]
            return jnp.einsum("ktab,ktbh->kah", weighted, picked)

        summed = lax.map(per_block, (one_tiles.reshape(VROWS, LB, TILES, TB, TB),
                                     one_table.reshape(VROWS, LB, TILES, TB),
                                     one_live.reshape(VROWS, LB, TILES)))
        return running + summed.reshape(V, width), None

    start_sum = jnp.zeros((V, width), jnp.float32)
    total, unused = lax.scan(per_relation, start_sum, (weight, tiles, table, live))
    root_term = jnp.dot(inputs, root, preferred_element_type=jnp.float32)
    return jax.nn.relu(total + root_term + bias).astype(jnp.bfloat16)


def reference(features, first_weight, first_root, first_bias, second_weight, second_root, second_bias, tiles, tile_source, tile_count, send_rows):
    table, live = source_table(tile_source, tile_count, send_rows)
    hidden = layer(features, first_weight, first_root, first_bias, tiles, table, live)
    result = layer(hidden, second_weight, second_root, second_bias, tiles, table, live)
    return result.reshape(VROWS, VDEV, HID)
```

```python
import jax
import jax.numpy as jnp
from jax import lax
from jax.sharding import PartitionSpec as P


GROUP = ("rel", "vcol")


def project(row_values, weight):
    return jnp.einsum("nf,sfh->nsh", row_values, weight, preferred_element_type=jnp.float32).astype(
        jnp.bfloat16
    )


def gather_blocks(sources, tile_source, block_size):
    block_count = sources.shape[0] // block_size
    blocks = sources.reshape(block_count, block_size, sources.shape[1], sources.shape[2])

    def pick(source_blocks, indices):
        return source_blocks[indices]

    return jax.vmap(pick, in_axes=(2, 0))(blocks, tile_source)


def aggregate(sources, masked, tile_source):
    picked = gather_blocks(sources, tile_source, masked.shape[-1])
    summed = jnp.einsum("sktab,sktbh->kah", masked, picked, preferred_element_type=jnp.float32)
    return summed.reshape(-1, summed.shape[-1])


def fetch_rows(values, send_index):
    outgoing = jnp.take(values, send_index, axis=0)
    return lax.all_to_all(outgoing, "vrow", split_axis=0, concat_axis=0, tiled=True)


def scatter_sum(part, parts):
    chunks = part.reshape(parts, part.shape[0] // parts, part.shape[1])
    received = lax.all_to_all(chunks, GROUP, 0, 0, tiled=False)
    return jnp.sum(received.astype(jnp.float32), axis=0)


def gather_all(share, parts):
    copies = jnp.broadcast_to(share[None], (parts,) + share.shape)
    received = lax.all_to_all(copies, GROUP, 0, 0, tiled=False)
    return received.reshape(parts * share.shape[0], share.shape[1])


def body(
    features,
    first_weight,
    first_root,
    first_bias,
    second_weight,
    second_root,
    second_bias,
    tiles,
    tile_source,
    tile_count,
    send_rows,
):
    local_rows = features.shape[0]
    send_index = send_rows.reshape(-1)
    tile_slots = tiles.shape[2]
    live_tiles = (jnp.arange(tile_slots, dtype=jnp.int32)[None, None, :] < tile_count).astype(
        tiles.dtype
    )
    masked = tiles * live_tiles[:, :, :, None, None]
    parts = lax.axis_size(GROUP)
    share_rows = local_rows // parts
    row_start = lax.axis_index(GROUP) * share_rows
    received = fetch_rows(features, send_index)
    first_proj = project(jnp.concatenate([features, received], axis=0), first_weight)
    first_part = aggregate(first_proj, masked, tile_source)
    first_share = scatter_sum(first_part.astype(jnp.bfloat16), parts)
    own_features = lax.dynamic_slice_in_dim(features, row_start, share_rows, 0)
    first_term = jnp.dot(own_features, first_root, preferred_element_type=jnp.float32)
    hidden_share = jax.nn.relu(first_share + first_term + first_bias).astype(jnp.bfloat16)
    hidden = gather_all(hidden_share, parts)
    received_hidden = fetch_rows(hidden, send_index)
    second_proj = project(jnp.concatenate([hidden, received_hidden], axis=0), second_weight)
    second_part = aggregate(second_proj, masked, tile_source)
    second_share = scatter_sum(second_part, parts)
    second_term = jnp.dot(hidden_share, second_root, preferred_element_type=jnp.float32)
    result = jax.nn.relu(second_share + second_term + second_bias).astype(jnp.bfloat16)
    return result[None]


def solution(mesh):
    in_specs = (
        P("vrow", None),
        P("rel", None, None),
        P(),
        P(),
        P("rel", None, None),
        P(),
        P(),
        P("rel", "vrow", "vcol", None, None),
        P("rel", "vrow", "vcol"),
        P("rel", "vrow", "vcol"),
        P("rel", "vrow", "vcol", None),
    )
    out_specs = P("vrow", GROUP, None)
    return jax.shard_map(body, mesh=mesh, in_specs=in_specs, out_specs=out_specs, check_vma=False)
```

```python
import jax
import jax.numpy as jnp
from jax import lax
from jax.sharding import PartitionSpec as P


GROUP = ("rel", "vcol")


def project(row_values, weight):
    return jnp.einsum("nf,sfh->nsh", row_values, weight, preferred_element_type=jnp.float32).astype(
        jnp.bfloat16
    )


def gather_blocks(sources, picks, block_size):
    block_count = sources.shape[0] // block_size
    blocks = sources.reshape(block_count, block_size, sources.shape[1], sources.shape[2])

    def pick(source_blocks, indices):
        return source_blocks[indices]

    return jax.vmap(pick, in_axes=(2, 0))(blocks, picks)


def aggregate(sources, weighted, picks):
    picked = gather_blocks(sources, picks, weighted.shape[-1])
    summed = jnp.einsum("sktab,sktbh->kah", weighted, picked, preferred_element_type=jnp.float32)
    return summed.reshape(-1, summed.shape[-1])


def layer_part(own_rows, far_rows, weight, local_tiles, remote_tiles, local_pick, remote_pick):
    own_proj = project(own_rows, weight)
    own_sum = aggregate(own_proj, local_tiles, local_pick)
    far_proj = project(far_rows, weight)
    return own_sum + aggregate(far_proj, remote_tiles, remote_pick)


def fetch_rows(values, send_index):
    outgoing = jnp.take(values, send_index, axis=0)
    return lax.all_to_all(outgoing, "vrow", split_axis=0, concat_axis=0, tiled=True)


def scatter_sum(part, parts):
    chunks = part.reshape(parts, part.shape[0] // parts, part.shape[1])
    received = lax.all_to_all(chunks, GROUP, 0, 0, tiled=False)
    return jnp.sum(received.astype(jnp.float32), axis=0)


def gather_all(share, parts):
    copies = jnp.broadcast_to(share[None], (parts,) + share.shape)
    received = lax.all_to_all(copies, GROUP, 0, 0, tiled=False)
    return received.reshape(parts * share.shape[0], share.shape[1])


def body(
    features,
    first_weight,
    first_root,
    first_bias,
    second_weight,
    second_root,
    second_bias,
    tiles,
    tile_source,
    tile_count,
    send_rows,
):
    local_rows = features.shape[0]
    send_index = send_rows.reshape(-1)
    tile_slots = tiles.shape[2]
    live_tiles = (jnp.arange(tile_slots, dtype=jnp.int32)[None, None, :] < tile_count).astype(
        tiles.dtype
    )
    masked = tiles * live_tiles[:, :, :, None, None]
    local_rows_blocks = local_rows // tiles.shape[-1]
    is_local = tile_source < local_rows_blocks
    local_tiles = masked * is_local.astype(tiles.dtype)[:, :, :, None, None]
    remote_tiles = masked * (~is_local).astype(tiles.dtype)[:, :, :, None, None]
    local_pick = jnp.where(is_local, tile_source, 0)
    remote_pick = jnp.where(is_local, 0, tile_source - local_rows_blocks)
    parts = lax.axis_size(GROUP)
    share_rows = local_rows // parts
    row_start = lax.axis_index(GROUP) * share_rows
    received = fetch_rows(features, send_index)
    first_part = layer_part(features, received, first_weight, local_tiles, remote_tiles, local_pick, remote_pick)
    first_share = scatter_sum(first_part.astype(jnp.bfloat16), parts)
    own_features = lax.dynamic_slice_in_dim(features, row_start, share_rows, 0)
    first_term = jnp.dot(own_features, first_root, preferred_element_type=jnp.float32)
    hidden_share = jax.nn.relu(first_share + first_term + first_bias).astype(jnp.bfloat16)
    hidden = gather_all(hidden_share, parts)
    received_hidden = fetch_rows(hidden, send_index)
    second_part = layer_part(hidden, received_hidden, second_weight, local_tiles, remote_tiles, local_pick, remote_pick)
    second_share = scatter_sum(second_part, parts)
    second_term = jnp.dot(hidden_share, second_root, preferred_element_type=jnp.float32)
    result = jax.nn.relu(second_share + second_term + second_bias).astype(jnp.bfloat16)
    return result[None]


def solution(mesh):
    in_specs = (
        P("vrow", None),
        P("rel", None, None),
        P(),
        P(),
        P("rel", None, None),
        P(),
        P(),
        P("rel", "vrow", "vcol", None, None),
        P("rel", "vrow", "vcol"),
        P("rel", "vrow", "vcol"),
        P("rel", "vrow", "vcol", None),
    )
    out_specs = P("vrow", GROUP, None)
    return jax.shard_map(body, mesh=mesh, in_specs=in_specs, out_specs=out_specs, check_vma=False)
```

```python
import jax
import jax.numpy as jnp
from jax import lax
from jax.sharding import PartitionSpec as P


GROUP = ("rel", "vcol")


def project(row_values, weight):
    return jnp.einsum("nf,sfh->nsh", row_values, weight, preferred_element_type=jnp.float32).astype(
        jnp.bfloat16
    )


def gather_blocks(sources, picks, block_size):
    block_count = sources.shape[0] // block_size
    blocks = sources.reshape(block_count, block_size, sources.shape[1], sources.shape[2])

    def pick(source_blocks, indices):
        return source_blocks[indices]

    return jax.vmap(pick, in_axes=(2, 0))(blocks, picks)


def aggregate(sources, weighted, picks):
    picked = gather_blocks(sources, picks, weighted.shape[-1])
    summed = jnp.einsum("sktab,sktbh->kah", weighted, picked, preferred_element_type=jnp.float32)
    return summed.reshape(-1, summed.shape[-1])


def layer_part(own_rows, far_rows, weight, local_tiles, remote_tiles, local_pick, remote_pick):
    own_proj = project(own_rows, weight)
    own_sum = aggregate(own_proj, local_tiles, local_pick)
    far_proj = project(far_rows, weight)
    return own_sum + aggregate(far_proj, remote_tiles, remote_pick)


def fetch_rows(values, send_index):
    outgoing = jnp.take(values, send_index, axis=0)
    return lax.all_to_all(outgoing, "vrow", split_axis=0, concat_axis=0, tiled=True)


def scatter_sum(part, parts):
    chunks = part.reshape(parts, part.shape[0] // parts, part.shape[1])
    received = lax.all_to_all(chunks, GROUP, 0, 0, tiled=False)
    return jnp.sum(received.astype(jnp.float32), axis=0)


def gather_all(share, parts):
    copies = jnp.broadcast_to(share[None], (parts,) + share.shape)
    received = lax.all_to_all(copies, GROUP, 0, 0, tiled=False)
    return received.reshape(parts * share.shape[0], share.shape[1])


def body(
    features,
    first_weight,
    first_root,
    first_bias,
    second_weight,
    second_root,
    second_bias,
    tiles,
    tile_source,
    tile_count,
    send_rows,
):
    local_rows = features.shape[0]
    send_index = send_rows.reshape(-1)
    tile_slots = tiles.shape[2]
    live_tiles = (jnp.arange(tile_slots, dtype=jnp.int32)[None, None, :] < tile_count).astype(
        tiles.dtype
    )
    masked = tiles * live_tiles[:, :, :, None, None]
    local_rows_blocks = local_rows // tiles.shape[-1]
    is_local = tile_source < local_rows_blocks
    local_tiles = masked * is_local.astype(tiles.dtype)[:, :, :, None, None]
    remote_tiles = masked * (~is_local).astype(tiles.dtype)[:, :, :, None, None]
    local_pick = jnp.where(is_local, tile_source, 0)
    remote_pick = jnp.where(is_local, 0, tile_source - local_rows_blocks)
    parts = lax.axis_size(GROUP)
    share_rows = local_rows // parts
    row_start = lax.axis_index(GROUP) * share_rows
    received = fetch_rows(features, send_index)
    first_part = layer_part(features, received, first_weight, local_tiles, remote_tiles, local_pick, remote_pick)
    first_share = scatter_sum(first_part.astype(jnp.bfloat16), parts)
    own_features = lax.dynamic_slice_in_dim(features, row_start, share_rows, 0)
    first_term = jnp.dot(own_features, first_root, preferred_element_type=jnp.float32)
    hidden_share = jax.nn.relu(first_share + first_term + first_bias).astype(jnp.bfloat16)
    hidden = gather_all(hidden_share, parts)
    received_hidden = fetch_rows(hidden, send_index)
    second_part = layer_part(hidden, received_hidden, second_weight, local_tiles, remote_tiles, local_pick, remote_pick)
    second_share = scatter_sum(second_part.astype(jnp.bfloat16), parts)
    second_term = jnp.dot(hidden_share, second_root, preferred_element_type=jnp.float32)
    result = jax.nn.relu(second_share + second_term + second_bias).astype(jnp.bfloat16)
    return result[None]


def solution(mesh):
    in_specs = (
        P("vrow", None),
        P("rel", None, None),
        P(),
        P(),
        P("rel", None, None),
        P(),
        P(),
        P("rel", "vrow", "vcol", None, None),
        P("rel", "vrow", "vcol"),
        P("rel", "vrow", "vcol"),
        P("rel", "vrow", "vcol", None),
    )
    out_specs = P("vrow", GROUP, None)
    return jax.shard_map(body, mesh=mesh, in_specs=in_specs, out_specs=out_specs, check_vma=False)
```

```python
import jax
import jax.numpy as jnp
from jax import lax
from jax.sharding import PartitionSpec as P


GROUP = ("rel", "vcol")


def project(row_values, weight):
    return jnp.einsum("nf,sfh->nsh", row_values, weight, preferred_element_type=jnp.float32).astype(
        jnp.bfloat16
    )


def gather_blocks(sources, picks, block_size):
    block_count = sources.shape[0] // block_size
    blocks = sources.reshape(block_count, block_size, sources.shape[1], sources.shape[2])

    def pick(source_blocks, indices):
        return source_blocks[indices]

    return jax.vmap(pick, in_axes=(2, 0))(blocks, picks)


def aggregate(sources, weighted, picks):
    picked = gather_blocks(sources, picks, weighted.shape[-1])
    summed = jnp.einsum("sktab,sktbh->kah", weighted, picked, preferred_element_type=jnp.float32)
    return summed.reshape(-1, summed.shape[-1])


def layer_part(own_rows, far_rows, weight, local_tiles, remote_tiles, local_pick, remote_pick):
    own_proj = project(own_rows, weight)
    own_sum = aggregate(own_proj, local_tiles, local_pick)
    far_proj = project(far_rows, weight)
    return own_sum + aggregate(far_proj, remote_tiles, remote_pick)


def fetch_rows(values, send_index):
    chooser = (send_index[:, None] == jnp.arange(values.shape[0], dtype=send_index.dtype)[None, :])
    outgoing = jnp.dot(chooser.astype(values.dtype), values, preferred_element_type=jnp.float32).astype(values.dtype)
    return lax.all_to_all(outgoing, "vrow", split_axis=0, concat_axis=0, tiled=True)


def scatter_sum(part, parts):
    chunks = part.reshape(parts, part.shape[0] // parts, part.shape[1])
    received = lax.all_to_all(chunks, GROUP, 0, 0, tiled=False)
    return jnp.sum(received.astype(jnp.float32), axis=0)


def gather_all(share, parts):
    copies = jnp.broadcast_to(share[None], (parts,) + share.shape)
    received = lax.all_to_all(copies, GROUP, 0, 0, tiled=False)
    return received.reshape(parts * share.shape[0], share.shape[1])


def body(
    features,
    first_weight,
    first_root,
    first_bias,
    second_weight,
    second_root,
    second_bias,
    tiles,
    tile_source,
    tile_count,
    send_rows,
):
    local_rows = features.shape[0]
    send_index = send_rows.reshape(-1)
    tile_slots = tiles.shape[2]
    live_tiles = (jnp.arange(tile_slots, dtype=jnp.int32)[None, None, :] < tile_count).astype(
        tiles.dtype
    )
    masked = tiles * live_tiles[:, :, :, None, None]
    local_rows_blocks = local_rows // tiles.shape[-1]
    is_local = tile_source < local_rows_blocks
    local_tiles = masked * is_local.astype(tiles.dtype)[:, :, :, None, None]
    remote_tiles = masked * (~is_local).astype(tiles.dtype)[:, :, :, None, None]
    local_pick = jnp.where(is_local, tile_source, 0)
    remote_pick = jnp.where(is_local, 0, tile_source - local_rows_blocks)
    parts = lax.axis_size(GROUP)
    share_rows = local_rows // parts
    row_start = lax.axis_index(GROUP) * share_rows
    received = fetch_rows(features, send_index)
    first_part = layer_part(features, received, first_weight, local_tiles, remote_tiles, local_pick, remote_pick)
    first_share = scatter_sum(first_part.astype(jnp.bfloat16), parts)
    own_features = lax.dynamic_slice_in_dim(features, row_start, share_rows, 0)
    first_term = jnp.dot(own_features, first_root, preferred_element_type=jnp.float32)
    hidden_share = jax.nn.relu(first_share + first_term + first_bias).astype(jnp.bfloat16)
    hidden = gather_all(hidden_share, parts)
    received_hidden = fetch_rows(hidden, send_index)
    second_part = layer_part(hidden, received_hidden, second_weight, local_tiles, remote_tiles, local_pick, remote_pick)
    second_share = scatter_sum(second_part.astype(jnp.bfloat16), parts)
    second_term = jnp.dot(hidden_share, second_root, preferred_element_type=jnp.float32)
    result = jax.nn.relu(second_share + second_term + second_bias).astype(jnp.bfloat16)
    return result[None]


def solution(mesh):
    in_specs = (
        P("vrow", None),
        P("rel", None, None),
        P(),
        P(),
        P("rel", None, None),
        P(),
        P(),
        P("rel", "vrow", "vcol", None, None),
        P("rel", "vrow", "vcol"),
        P("rel", "vrow", "vcol"),
        P("rel", "vrow", "vcol", None),
    )
    out_specs = P("vrow", GROUP, None)
    return jax.shard_map(body, mesh=mesh, in_specs=in_specs, out_specs=out_specs, check_vma=False)
```

```python
import jax
import jax.numpy as jnp
from jax import lax
from jax.sharding import PartitionSpec as P


GROUP = ("rel", "vcol")


def project(row_values, weight):
    return jnp.einsum("nf,sfh->nsh", row_values, weight, preferred_element_type=jnp.float32).astype(
        jnp.bfloat16
    )


def gather_blocks(sources, picks, block_size):
    block_count = sources.shape[0] // block_size
    blocks = sources.reshape(block_count, block_size, sources.shape[1], sources.shape[2])

    def pick(source_blocks, indices):
        return source_blocks[indices]

    return jax.vmap(pick, in_axes=(2, 0))(blocks, picks)


def aggregate(sources, weighted, picks):
    picked = gather_blocks(sources, picks, weighted.shape[-1])
    summed = jnp.einsum("sktab,sktbh->kah", weighted, picked, preferred_element_type=jnp.float32)
    return summed.reshape(-1, summed.shape[-1])


def far_aggregate(far_proj, remote_dense):
    blocks = remote_dense.shape[3]
    rows = far_proj.reshape(blocks, far_proj.shape[0] // blocks, far_proj.shape[1], far_proj.shape[2])
    summed = jnp.einsum("rkasb,sbrh->kah", remote_dense, rows.astype(jnp.float32),
                        precision=lax.Precision.HIGHEST, preferred_element_type=jnp.float32)
    return summed.reshape(-1, summed.shape[-1])


def layer_part(own_rows, far_rows, weight, local_tiles, remote_dense, local_pick):
    own_proj = project(own_rows, weight)
    own_sum = aggregate(own_proj, local_tiles, local_pick)
    far_proj = project(far_rows, weight)
    return own_sum + far_aggregate(far_proj, remote_dense)


def fetch_rows(values, send_index):
    chooser = (send_index[:, None] == jnp.arange(values.shape[0], dtype=send_index.dtype)[None, :])
    outgoing = jnp.dot(chooser.astype(values.dtype), values, preferred_element_type=jnp.float32).astype(values.dtype)
    return lax.all_to_all(outgoing, "vrow", split_axis=0, concat_axis=0, tiled=True)


def scatter_sum(part, parts):
    chunks = part.reshape(parts, part.shape[0] // parts, part.shape[1])
    received = lax.all_to_all(chunks, GROUP, 0, 0, tiled=False)
    return jnp.sum(received.astype(jnp.float32), axis=0)


def gather_all(share, parts):
    copies = jnp.broadcast_to(share[None], (parts,) + share.shape)
    received = lax.all_to_all(copies, GROUP, 0, 0, tiled=False)
    return received.reshape(parts * share.shape[0], share.shape[1])


def body(
    features,
    first_weight,
    first_root,
    first_bias,
    second_weight,
    second_root,
    second_bias,
    tiles,
    tile_source,
    tile_count,
    send_rows,
):
    local_rows = features.shape[0]
    send_index = send_rows.reshape(-1)
    tile_slots = tiles.shape[2]
    live_tiles = (jnp.arange(tile_slots, dtype=jnp.int32)[None, None, :] < tile_count).astype(
        tiles.dtype
    )
    masked = tiles * live_tiles[:, :, :, None, None]
    local_rows_blocks = local_rows // tiles.shape[-1]
    is_local = tile_source < local_rows_blocks
    local_tiles = masked * is_local.astype(tiles.dtype)[:, :, :, None, None]
    remote_tiles = masked * (~is_local).astype(tiles.dtype)[:, :, :, None, None]
    local_pick = jnp.where(is_local, tile_source, 0)
    remote_pick = jnp.where(is_local, -1, tile_source - local_rows_blocks)
    remote_blocks = send_index.shape[0] // tiles.shape[-1]
    remote_choice = (remote_pick[..., None] == jnp.arange(remote_blocks, dtype=remote_pick.dtype)).astype(jnp.float32)
    remote_dense = jnp.einsum("rktab,rkts->rkasb", remote_tiles.astype(jnp.float32), remote_choice,
                              precision=lax.Precision.HIGHEST)
    parts = lax.axis_size(GROUP)
    share_rows = local_rows // parts
    row_start = lax.axis_index(GROUP) * share_rows
    received = fetch_rows(features, send_index)
    first_part = layer_part(features, received, first_weight, local_tiles, remote_dense, local_pick)
    first_share = scatter_sum(first_part.astype(jnp.bfloat16), parts)
    own_features = lax.dynamic_slice_in_dim(features, row_start, share_rows, 0)
    first_term = jnp.dot(own_features, first_root, preferred_element_type=jnp.float32)
    hidden_share = jax.nn.relu(first_share + first_term + first_bias).astype(jnp.bfloat16)
    hidden = gather_all(hidden_share, parts)
    received_hidden = fetch_rows(hidden, send_index)
    second_part = layer_part(hidden, received_hidden, second_weight, local_tiles, remote_dense, local_pick)
    second_share = scatter_sum(second_part.astype(jnp.bfloat16), parts)
    second_term = jnp.dot(hidden_share, second_root, preferred_element_type=jnp.float32)
    result = jax.nn.relu(second_share + second_term + second_bias).astype(jnp.bfloat16)
    return result[None]


def solution(mesh):
    in_specs = (
        P("vrow", None),
        P("rel", None, None),
        P(),
        P(),
        P("rel", None, None),
        P(),
        P(),
        P("rel", "vrow", "vcol", None, None),
        P("rel", "vrow", "vcol"),
        P("rel", "vrow", "vcol"),
        P("rel", "vrow", "vcol", None),
    )
    out_specs = P("vrow", GROUP, None)
    return jax.shard_map(body, mesh=mesh, in_specs=in_specs, out_specs=out_specs, check_vma=False)
```

```python
import jax
import jax.numpy as jnp
from jax import lax
from jax.sharding import PartitionSpec as P


GROUP = ("rel", "vcol")


def project(row_values, weight):
    return jnp.einsum("nf,sfh->nsh", row_values, weight, preferred_element_type=jnp.float32).astype(
        jnp.bfloat16
    )


def gather_blocks(sources, picks, block_size):
    block_count = sources.shape[0] // block_size
    blocks = sources.reshape(block_count, block_size, sources.shape[1], sources.shape[2])

    def pick(source_blocks, indices):
        return source_blocks[indices]

    return jax.vmap(pick, in_axes=(2, 0))(blocks, picks)


def aggregate(sources, weighted, picks):
    picked = gather_blocks(sources, picks, weighted.shape[-1])
    summed = jnp.einsum("sktab,sktbh->kah", weighted, picked, preferred_element_type=jnp.float32)
    return summed.reshape(-1, summed.shape[-1])


def far_aggregate(far_proj, remote_dense):
    blocks = remote_dense.shape[3]
    rows = far_proj.reshape(blocks, far_proj.shape[0] // blocks, far_proj.shape[1], far_proj.shape[2])
    summed = jnp.einsum("rkasb,sbrh->kah", remote_dense, rows.astype(jnp.float32),
                        precision=lax.Precision.HIGHEST, preferred_element_type=jnp.float32)
    return summed.reshape(-1, summed.shape[-1])


def layer_part(own_rows, far_rows, weight, local_tiles, remote_dense, local_pick):
    own_proj = project(own_rows, weight)
    own_sum = aggregate(own_proj, local_tiles, local_pick)
    far_proj = project(far_rows, weight)
    return own_sum + far_aggregate(far_proj, remote_dense)


def fetch_rows(values, send_index):
    chooser = (send_index[:, None] == jnp.arange(values.shape[0], dtype=send_index.dtype)[None, :])
    outgoing = jnp.dot(chooser.astype(values.dtype), values, preferred_element_type=values.dtype)
    return lax.all_to_all(outgoing, "vrow", split_axis=0, concat_axis=0, tiled=True)


def scatter_sum(part, parts):
    chunks = part.reshape(parts, part.shape[0] // parts, part.shape[1])
    received = lax.all_to_all(chunks, GROUP, 0, 0, tiled=False)
    return jnp.sum(received.astype(jnp.float32), axis=0)


def gather_all(share, parts):
    copies = jnp.broadcast_to(share[None], (parts,) + share.shape)
    received = lax.all_to_all(copies, GROUP, 0, 0, tiled=False)
    return received.reshape(parts * share.shape[0], share.shape[1])


def body(
    features,
    first_weight,
    first_root,
    first_bias,
    second_weight,
    second_root,
    second_bias,
    tiles,
    tile_source,
    tile_count,
    send_rows,
):
    local_rows = features.shape[0]
    send_index = send_rows.reshape(-1)
    tile_slots = tiles.shape[2]
    live_tiles = (jnp.arange(tile_slots, dtype=jnp.int32)[None, None, :] < tile_count).astype(
        tiles.dtype
    )
    masked = tiles * live_tiles[:, :, :, None, None]
    local_rows_blocks = local_rows // tiles.shape[-1]
    is_local = tile_source < local_rows_blocks
    local_tiles = masked * is_local.astype(tiles.dtype)[:, :, :, None, None]
    remote_tiles = masked * (~is_local).astype(tiles.dtype)[:, :, :, None, None]
    local_pick = jnp.where(is_local, tile_source, 0)
    remote_pick = jnp.where(is_local, -1, tile_source - local_rows_blocks)
    remote_blocks = send_index.shape[0] // tiles.shape[-1]
    remote_choice = (remote_pick[..., None] == jnp.arange(remote_blocks, dtype=remote_pick.dtype)).astype(jnp.float32)
    remote_dense = jnp.einsum("rktab,rkts->rkasb", remote_tiles.astype(jnp.float32), remote_choice,
                              precision=lax.Precision.HIGHEST)
    parts = lax.axis_size(GROUP)
    share_rows = local_rows // parts
    row_start = lax.axis_index(GROUP) * share_rows
    received = fetch_rows(features, send_index)
    first_part = layer_part(features, received, first_weight, local_tiles, remote_dense, local_pick)
    first_share = scatter_sum(first_part.astype(jnp.bfloat16), parts)
    own_features = lax.dynamic_slice_in_dim(features, row_start, share_rows, 0)
    first_term = jnp.dot(own_features, first_root, preferred_element_type=jnp.float32)
    hidden_share = jax.nn.relu(first_share + first_term + first_bias).astype(jnp.bfloat16)
    hidden = gather_all(hidden_share, parts)
    received_hidden = fetch_rows(hidden, send_index)
    second_part = layer_part(hidden, received_hidden, second_weight, local_tiles, remote_dense, local_pick)
    second_share = scatter_sum(second_part.astype(jnp.bfloat16), parts)
    second_term = jnp.dot(hidden_share, second_root, preferred_element_type=jnp.float32)
    result = jax.nn.relu(second_share + second_term + second_bias).astype(jnp.bfloat16)
    return result[None]


def solution(mesh):
    in_specs = (
        P("vrow", None),
        P("rel", None, None),
        P(),
        P(),
        P("rel", None, None),
        P(),
        P(),
        P("rel", "vrow", "vcol", None, None),
        P("rel", "vrow", "vcol"),
        P("rel", "vrow", "vcol"),
        P("rel", "vrow", "vcol", None),
    )
    out_specs = P("vrow", GROUP, None)
    return jax.shard_map(body, mesh=mesh, in_specs=in_specs, out_specs=out_specs, check_vma=False)
```

```python
import jax
import jax.numpy as jnp
from jax import lax
from jax.sharding import PartitionSpec as P


GROUP = ("rel", "vcol")


def project(row_values, weight):
    return jnp.einsum("nf,sfh->nsh", row_values, weight, preferred_element_type=jnp.float32).astype(
        jnp.bfloat16
    )


def gather_blocks(sources, picks, block_size):
    block_count = sources.shape[0] // block_size
    blocks = sources.reshape(block_count, block_size, sources.shape[1], sources.shape[2])

    def pick(source_blocks, indices):
        return source_blocks[indices]

    return jax.vmap(pick, in_axes=(2, 0))(blocks, picks)


def aggregate(sources, weighted, picks):
    picked = gather_blocks(sources, picks, weighted.shape[-1])
    summed = jnp.einsum("sktab,sktbh->kah", weighted, picked, preferred_element_type=jnp.float32)
    return summed.reshape(-1, summed.shape[-1])


def far_aggregate(far_proj, remote_dense):
    blocks = remote_dense.shape[3]
    rows = far_proj.reshape(blocks, far_proj.shape[0] // blocks, far_proj.shape[1], far_proj.shape[2])
    summed = jnp.einsum("rkasb,sbrh->kah", remote_dense, rows.astype(jnp.float32),
                        precision=lax.Precision.HIGH, preferred_element_type=jnp.float32)
    return summed.reshape(-1, summed.shape[-1])


def layer_part(own_rows, far_rows, weight, local_tiles, remote_dense, local_pick):
    own_proj = project(own_rows, weight)
    own_sum = aggregate(own_proj, local_tiles, local_pick)
    far_proj = project(far_rows, weight)
    return own_sum + far_aggregate(far_proj, remote_dense)


def fetch_rows(values, send_index):
    chooser = (send_index[:, None] == jnp.arange(values.shape[0], dtype=send_index.dtype)[None, :])
    outgoing = jnp.dot(chooser.astype(values.dtype), values, preferred_element_type=jnp.float32).astype(values.dtype)
    return lax.all_to_all(outgoing, "vrow", split_axis=0, concat_axis=0, tiled=True)


def scatter_sum(part, parts):
    chunks = part.reshape(parts, part.shape[0] // parts, part.shape[1])
    received = lax.all_to_all(chunks, GROUP, 0, 0, tiled=False)
    return jnp.sum(received.astype(jnp.float32), axis=0)


def gather_all(share, parts):
    copies = jnp.broadcast_to(share[None], (parts,) + share.shape)
    received = lax.all_to_all(copies, GROUP, 0, 0, tiled=False)
    return received.reshape(parts * share.shape[0], share.shape[1])


def body(
    features,
    first_weight,
    first_root,
    first_bias,
    second_weight,
    second_root,
    second_bias,
    tiles,
    tile_source,
    tile_count,
    send_rows,
):
    local_rows = features.shape[0]
    send_index = send_rows.reshape(-1)
    tile_slots = tiles.shape[2]
    live_tiles = (jnp.arange(tile_slots, dtype=jnp.int32)[None, None, :] < tile_count).astype(
        tiles.dtype
    )
    masked = tiles * live_tiles[:, :, :, None, None]
    local_rows_blocks = local_rows // tiles.shape[-1]
    is_local = tile_source < local_rows_blocks
    local_tiles = masked * is_local.astype(tiles.dtype)[:, :, :, None, None]
    remote_tiles = masked * (~is_local).astype(tiles.dtype)[:, :, :, None, None]
    local_pick = jnp.where(is_local, tile_source, 0)
    remote_pick = jnp.where(is_local, -1, tile_source - local_rows_blocks)
    remote_blocks = send_index.shape[0] // tiles.shape[-1]
    remote_choice = (remote_pick[..., None] == jnp.arange(remote_blocks, dtype=remote_pick.dtype)).astype(jnp.float32)
    remote_dense = jnp.einsum("rktab,rkts->rkasb", remote_tiles.astype(jnp.float32), remote_choice,
                              precision=lax.Precision.HIGHEST)
    parts = lax.axis_size(GROUP)
    share_rows = local_rows // parts
    row_start = lax.axis_index(GROUP) * share_rows
    received = fetch_rows(features, send_index)
    first_part = layer_part(features, received, first_weight, local_tiles, remote_dense, local_pick)
    first_share = scatter_sum(first_part.astype(jnp.bfloat16), parts)
    own_features = lax.dynamic_slice_in_dim(features, row_start, share_rows, 0)
    first_term = lax.optimization_barrier(jnp.dot(own_features, first_root, preferred_element_type=jnp.float32) + first_bias)
    hidden_share = jax.nn.relu(first_share + first_term).astype(jnp.bfloat16)
    hidden = gather_all(hidden_share, parts)
    received_hidden = fetch_rows(hidden, send_index)
    second_part = layer_part(hidden, received_hidden, second_weight, local_tiles, remote_dense, local_pick)
    second_share = scatter_sum(second_part.astype(jnp.bfloat16), parts)
    second_term = lax.optimization_barrier(jnp.dot(hidden_share, second_root, preferred_element_type=jnp.float32) + second_bias)
    result = jax.nn.relu(second_share + second_term).astype(jnp.bfloat16)
    return result[None]


def solution(mesh):
    in_specs = (
        P("vrow", None),
        P("rel", None, None),
        P(),
        P(),
        P("rel", None, None),
        P(),
        P(),
        P("rel", "vrow", "vcol", None, None),
        P("rel", "vrow", "vcol"),
        P("rel", "vrow", "vcol"),
        P("rel", "vrow", "vcol", None),
    )
    out_specs = P("vrow", GROUP, None)
    return jax.shard_map(body, mesh=mesh, in_specs=in_specs, out_specs=out_specs, check_vma=False)
```

```python
import jax
import jax.numpy as jnp
from jax import lax
from jax.sharding import PartitionSpec as P


GROUP = ("rel", "vcol")


def project(row_values, weight):
    return jnp.einsum("nf,sfh->nsh", row_values, weight, preferred_element_type=jnp.float32).astype(
        jnp.bfloat16
    )


def gather_blocks(sources, picks, block_size):
    block_count = sources.shape[0] // block_size
    blocks = sources.reshape(block_count, block_size, sources.shape[1], sources.shape[2])

    def pick(source_blocks, indices):
        return source_blocks[indices]

    return jax.vmap(pick, in_axes=(2, 0))(blocks, picks)


def aggregate(sources, weighted, picks):
    picked = gather_blocks(sources, picks, weighted.shape[-1])
    summed = jnp.einsum("sktab,sktbh->kah", weighted, picked, preferred_element_type=jnp.float32)
    return summed.reshape(-1, summed.shape[-1])


def far_aggregate(far_proj, remote_dense):
    blocks = remote_dense.shape[3]
    rows = far_proj.reshape(blocks, far_proj.shape[0] // blocks, far_proj.shape[1], far_proj.shape[2])
    summed = jnp.einsum("rkasb,sbrh->kah", remote_dense, rows.astype(jnp.float32),
                        precision=lax.Precision.HIGH, preferred_element_type=jnp.float32)
    return summed.reshape(-1, summed.shape[-1])


def layer_part(own_rows, far_rows, weight, local_tiles, remote_dense, local_pick):
    own_proj = project(own_rows, weight)
    own_sum = aggregate(own_proj, local_tiles, local_pick)
    far_proj = project(far_rows, weight)
    return own_sum + far_aggregate(far_proj, remote_dense)


def fetch_rows(values, chooser):
    outgoing = jnp.dot(chooser, values, preferred_element_type=jnp.float32).astype(values.dtype)
    return lax.all_to_all(outgoing, "vrow", split_axis=0, concat_axis=0, tiled=True)


def scatter_sum(part, parts):
    chunks = part.reshape(parts, part.shape[0] // parts, part.shape[1])
    received = lax.all_to_all(chunks, GROUP, 0, 0, tiled=False)
    return jnp.sum(received.astype(jnp.float32), axis=0)


def gather_all(share, parts):
    copies = jnp.broadcast_to(share[None], (parts,) + share.shape)
    received = lax.all_to_all(copies, GROUP, 0, 0, tiled=False)
    return received.reshape(parts * share.shape[0], share.shape[1])


def body(
    features,
    first_weight,
    first_root,
    first_bias,
    second_weight,
    second_root,
    second_bias,
    tiles,
    tile_source,
    tile_count,
    send_rows,
):
    local_rows = features.shape[0]
    send_index = send_rows.reshape(-1)
    tile_slots = tiles.shape[2]
    live_tiles = (jnp.arange(tile_slots, dtype=jnp.int32)[None, None, :] < tile_count).astype(
        tiles.dtype
    )
    masked = tiles * live_tiles[:, :, :, None, None]
    local_rows_blocks = local_rows // tiles.shape[-1]
    is_local = tile_source < local_rows_blocks
    local_tiles = masked * is_local.astype(tiles.dtype)[:, :, :, None, None]
    remote_tiles = masked * (~is_local).astype(tiles.dtype)[:, :, :, None, None]
    local_pick = jnp.where(is_local, tile_source, 0)
    remote_pick = jnp.where(is_local, -1, tile_source - local_rows_blocks)
    remote_blocks = send_index.shape[0] // tiles.shape[-1]
    remote_choice = (remote_pick[..., None] == jnp.arange(remote_blocks, dtype=remote_pick.dtype)).astype(jnp.float32)
    remote_dense = jnp.einsum("rktab,rkts->rkasb", remote_tiles.astype(jnp.float32), remote_choice,
                              precision=lax.Precision.HIGHEST)
    parts = lax.axis_size(GROUP)
    share_rows = local_rows // parts
    row_start = lax.axis_index(GROUP) * share_rows
    chooser = send_index[:, None] == jnp.arange(local_rows, dtype=send_index.dtype)[None, :]
    chooser = lax.optimization_barrier(chooser.astype(features.dtype))
    received = fetch_rows(features, chooser)
    first_part = layer_part(features, received, first_weight, local_tiles, remote_dense, local_pick)
    first_share = scatter_sum(first_part.astype(jnp.bfloat16), parts)
    own_features = lax.dynamic_slice_in_dim(features, row_start, share_rows, 0)
    first_term = lax.optimization_barrier(jnp.dot(own_features, first_root, preferred_element_type=jnp.float32) + first_bias)
    hidden_share = jax.nn.relu(first_share + first_term).astype(jnp.bfloat16)
    hidden = gather_all(hidden_share, parts)
    received_hidden = fetch_rows(hidden, chooser)
    second_part = layer_part(hidden, received_hidden, second_weight, local_tiles, remote_dense, local_pick)
    second_share = scatter_sum(second_part.astype(jnp.bfloat16), parts)
    second_term = lax.optimization_barrier(jnp.dot(hidden_share, second_root, preferred_element_type=jnp.float32) + second_bias)
    result = jax.nn.relu(second_share + second_term).astype(jnp.bfloat16)
    return result[None]


def solution(mesh):
    in_specs = (
        P("vrow", None),
        P("rel", None, None),
        P(),
        P(),
        P("rel", None, None),
        P(),
        P(),
        P("rel", "vrow", "vcol", None, None),
        P("rel", "vrow", "vcol"),
        P("rel", "vrow", "vcol"),
        P("rel", "vrow", "vcol", None),
    )
    out_specs = P("vrow", GROUP, None)
    return jax.shard_map(body, mesh=mesh, in_specs=in_specs, out_specs=out_specs, check_vma=False)
```

```python
import jax
import jax.numpy as jnp
from jax import lax
from jax.sharding import PartitionSpec as P


GROUP = ("rel", "vcol")


def project(row_values, weight):
    return jnp.einsum("nf,sfh->nsh", row_values, weight, preferred_element_type=jnp.float32).astype(
        jnp.bfloat16
    )


def gather_blocks(sources, picks, block_size):
    block_count = sources.shape[0] // block_size
    blocks = sources.reshape(block_count, block_size, sources.shape[1], sources.shape[2])

    def pick(source_blocks, indices):
        return source_blocks[indices]

    return jax.vmap(pick, in_axes=(2, 0))(blocks, picks)


def aggregate(sources, weighted, picks):
    picked = gather_blocks(sources, picks, weighted.shape[-1])
    summed = jnp.einsum("sktab,sktbh->kah", weighted, picked, preferred_element_type=jnp.float32)
    return summed.reshape(-1, summed.shape[-1])


def far_aggregate(far_proj, remote_dense):
    blocks = remote_dense.shape[3]
    rows = far_proj.reshape(blocks, far_proj.shape[0] // blocks, far_proj.shape[1], far_proj.shape[2])
    summed = jnp.einsum("rkasb,sbrh->kah", remote_dense, rows.astype(jnp.float32),
                        preferred_element_type=jnp.float32)
    return summed.reshape(-1, summed.shape[-1])


def layer_part(own_rows, far_rows, weight, local_tiles, remote_dense, local_pick):
    own_proj = project(own_rows, weight)
    own_sum = aggregate(own_proj, local_tiles, local_pick)
    far_proj = project(far_rows, weight)
    return own_sum + far_aggregate(far_proj, remote_dense)


def fetch_rows(values, send_index):
    chooser = (send_index[:, None] == jnp.arange(values.shape[0], dtype=send_index.dtype)[None, :])
    outgoing = jnp.dot(chooser.astype(values.dtype), values, preferred_element_type=jnp.float32).astype(values.dtype)
    return lax.all_to_all(outgoing, "vrow", split_axis=0, concat_axis=0, tiled=True)


def scatter_sum(part, parts):
    chunks = part.reshape(parts, part.shape[0] // parts, part.shape[1])
    received = lax.all_to_all(chunks, GROUP, 0, 0, tiled=False)
    return jnp.sum(received.astype(jnp.float32), axis=0)


def gather_all(share, parts):
    copies = jnp.broadcast_to(share[None], (parts,) + share.shape)
    received = lax.all_to_all(copies, GROUP, 0, 0, tiled=False)
    return received.reshape(parts * share.shape[0], share.shape[1])


def body(
    features,
    first_weight,
    first_root,
    first_bias,
    second_weight,
    second_root,
    second_bias,
    tiles,
    tile_source,
    tile_count,
    send_rows,
):
    local_rows = features.shape[0]
    send_index = send_rows.reshape(-1)
    tile_slots = tiles.shape[2]
    live_tiles = (jnp.arange(tile_slots, dtype=jnp.int32)[None, None, :] < tile_count).astype(
        tiles.dtype
    )
    masked = tiles * live_tiles[:, :, :, None, None]
    local_rows_blocks = local_rows // tiles.shape[-1]
    is_local = tile_source < local_rows_blocks
    local_tiles = masked * is_local.astype(tiles.dtype)[:, :, :, None, None]
    remote_tiles = masked * (~is_local).astype(tiles.dtype)[:, :, :, None, None]
    local_pick = jnp.where(is_local, tile_source, 0)
    remote_pick = jnp.where(is_local, -1, tile_source - local_rows_blocks)
    remote_blocks = send_index.shape[0] // tiles.shape[-1]
    remote_choice = (remote_pick[..., None] == jnp.arange(remote_blocks, dtype=remote_pick.dtype)).astype(jnp.float32)
    remote_dense = jnp.einsum("rktab,rkts->rkasb", remote_tiles.astype(jnp.float32), remote_choice,
                              precision=lax.Precision.HIGHEST)
    parts = lax.axis_size(GROUP)
    share_rows = local_rows // parts
    row_start = lax.axis_index(GROUP) * share_rows
    received = fetch_rows(features, send_index)
    first_part = layer_part(features, received, first_weight, local_tiles, remote_dense, local_pick)
    first_share = scatter_sum(first_part.astype(jnp.bfloat16), parts)
    own_features = lax.dynamic_slice_in_dim(features, row_start, share_rows, 0)
    first_term = lax.optimization_barrier(jnp.dot(own_features, first_root, preferred_element_type=jnp.float32) + first_bias)
    hidden_share = jax.nn.relu(first_share + first_term).astype(jnp.bfloat16)
    hidden = gather_all(hidden_share, parts)
    received_hidden = fetch_rows(hidden, send_index)
    second_part = layer_part(hidden, received_hidden, second_weight, local_tiles, remote_dense, local_pick)
    second_share = scatter_sum(second_part.astype(jnp.bfloat16), parts)
    second_term = lax.optimization_barrier(jnp.dot(hidden_share, second_root, preferred_element_type=jnp.float32) + second_bias)
    result = jax.nn.relu(second_share + second_term).astype(jnp.bfloat16)
    return result[None]


def solution(mesh):
    in_specs = (
        P("vrow", None),
        P("rel", None, None),
        P(),
        P(),
        P("rel", None, None),
        P(),
        P(),
        P("rel", "vrow", "vcol", None, None),
        P("rel", "vrow", "vcol"),
        P("rel", "vrow", "vcol"),
        P("rel", "vrow", "vcol", None),
    )
    out_specs = P("vrow", GROUP, None)
    return jax.shard_map(body, mesh=mesh, in_specs=in_specs, out_specs=out_specs, check_vma=False)
```
